512 devices in a mesh: chan: 32 (over y_hi, x, core), tm: 16 (over y_lo, z).
Axes of the slice: x: 4, y: 8 (y_hi: 4, y_lo: 2; y = y_hi * 2 + y_lo), z: 8, core: 2. Of those that a mesh axis runs over, the one named last changes fastest.
Arguments:
- raw_strain: float32 [2048, 16384], P('chan', 'tm'), may hold values from -2000 to 2000
- fir_taps: float32 [64], replicated, may hold values from -0.75 to 0.75
- block_mask: int32 [32, 32], replicated, may hold values 0 or 1
Outputs:
- correlations: float32 [128, 2048, 2048], P('tm', 'chan')
The draws below stay inside these ranges and needn't reach their ends.
All inputs are finite; a program needn't handle non-finite values.
Results may differ from the reference program's by a relative error of at most 0.0054.
Values may be sent and summed in bfloat16 or wider, within the bound.
No kernel may reach another device: no remote copies, remote signals or barrier semaphores. Data moves between devices by JAX's collectives and lax.ppermute only.
A program may use at most 64 MiB of HBM per device.

```python
import math
import jax
import jax.numpy as jnp
from jax import lax

CHAN_DEV = 64
DECIM = 8
TAPS = 64
LAGS = 128
CHANNELS = 2048
BLOCKS = 32
SAMPLES = 2048
RAW = 16384


def draw_raw_strain(key, part):
    key_scale, key_noise = jax.random.split(key, 2)
    channel_scale = jnp.exp(jax.random.uniform(key_scale, (CHANNELS, 1), jnp.float32) * math.log(10.0))
    position = jnp.arange(RAW, dtype=jnp.float32)[None, :] / RAW
    base = jnp.clip(jax.random.normal(key_noise, (CHANNELS, RAW), jnp.float32), -6.0, 6.0)
    envelope = jnp.exp(math.log(10.0) * position)
    return (channel_scale * envelope * base).astype(jnp.float32)


def with_ends(entries, rng, least, largest):
    longest = entries.shape.index(max(entries.shape))
    spots = []
    for shift in (0, 1):
        where = [jax.random.randint(jax.random.fold_in(rng, axis), (), 0, length) for axis, length in enumerate(entries.shape)]
        where[longest] = (where[longest] + shift) % entries.shape[longest]
        spots.append(tuple(where))
    return entries.at[spots[0]].set(least).at[spots[1]].set(largest)


def scatter_about(rng, extent, spread, limit, kind=jnp.bfloat16):
    result = jax.random.normal(rng, extent, jnp.float32) * spread
    return jnp.minimum(jnp.maximum(result, -limit), limit).astype(kind)


def setup_inputs(seed: int = 0) -> dict:
    keys = jax.random.split(jax.random.key(seed), 4)
    raw_strain = draw_raw_strain(jax.random.fold_in(keys[3], 71), 0)
    fir_taps = scatter_about(keys[1], (TAPS,), TAPS ** -0.5, 0.75, jnp.float32)
    block_mask = with_ends((jax.random.randint(keys[2], (BLOCKS, BLOCKS), 0, 2) < 1).astype(jnp.int32), jax.random.fold_in(keys[2], 1), 0, 1)
    return dict(raw_strain=raw_strain, fir_taps=fir_taps, block_mask=block_mask)


def reference(raw_strain, fir_taps, block_mask):
    margin = TAPS - DECIM
    padded = jnp.pad(raw_strain, ((0, 0), (margin, 0)))
    decimated = jnp.zeros((CHANNELS, SAMPLES), jnp.float32)
    for tap_index in range(TAPS):
        begin = margin + DECIM - 1 - tap_index
        strided = lax.slice_in_dim(padded, begin, begin + DECIM * (SAMPLES - 1) + 1, DECIM, 1)
        decimated = decimated + fir_taps[tap_index] * strided
    rounded = decimated.astype(jnp.bfloat16)
    float_values = rounded.astype(jnp.float32)
    root_mean = jnp.sqrt(lax.optimization_barrier(jnp.mean(float_values * float_values, axis=1, keepdims=True)) + 1e-06)
    whitened = (float_values / root_mean).astype(jnp.bfloat16)
    wide_values = whitened.astype(jnp.float32)
    wide_padded = jnp.pad(wide_values, ((0, 0), (0, LAGS)))
    mask_full = jnp.repeat(jnp.repeat(block_mask, CHAN_DEV, axis=0), CHAN_DEV, axis=1)
    weights = mask_full.astype(jnp.float32) * (1.0 / math.sqrt(SAMPLES))

    def one_lag(lag_index):
        shifted = lax.dynamic_slice_in_dim(wide_padded, lag_index, SAMPLES, 1)
        product = jnp.dot(wide_values, shifted.T, precision=lax.Precision.HIGHEST, preferred_element_type=jnp.float32)
        return product * weights
    return lax.map(one_lag, jnp.arange(LAGS, dtype=jnp.int32))
```

```python
import math

import jax
import jax.numpy as jnp
from jax import lax
from jax.sharding import PartitionSpec as P

DECIM = 8
TAPS = 64
LAGS = 128


def from_behind(value, axis, steps):
    count = lax.axis_size(axis)
    first, last = (max(0, -steps), min(count, count - steps))
    return lax.ppermute(value, axis, [(source, source + steps) for source in range(first, last)])


def decimate(raw_strain, fir_taps):
    time_span = raw_strain.shape[1]
    margin = TAPS - DECIM
    earlier = from_behind(raw_strain[:, time_span - margin :], "tm", 1)
    extended = jnp.concatenate([earlier, raw_strain], axis=1)
    outputs = time_span // DECIM
    tap_blocks = TAPS // DECIM
    frames = outputs + tap_blocks - 1
    tap_table = fir_taps[::-1].reshape(tap_blocks, DECIM)
    shape_three = (frames, outputs, tap_blocks)
    matches = lax.broadcasted_iota(jnp.int32, shape_three, 0) - lax.broadcasted_iota(
        jnp.int32, shape_three, 1
    ) == lax.broadcasted_iota(jnp.int32, shape_three, 2)
    one_hot = matches.astype(jnp.float32)
    filter_matrix = jnp.einsum("mtj,jr->mrt", one_hot, tap_table, precision=lax.Precision.HIGHEST)
    filter_matrix = filter_matrix.reshape(frames * DECIM, outputs)
    return jnp.dot(
        extended, filter_matrix, precision=lax.Precision.HIGHEST, preferred_element_type=jnp.float32
    )


def per_device(raw_strain, fir_taps, block_mask):
    channel_rows = raw_strain.shape[0]
    chan_parts = lax.axis_size("chan")
    tm_parts = lax.axis_size("tm")
    decimated = decimate(raw_strain, fir_taps)
    rounded = decimated.astype(jnp.bfloat16)
    local_span = rounded.shape[1]
    samples = local_span * tm_parts
    values = rounded.astype(jnp.float32)
    square_sum = lax.psum(jnp.sum(values * values, axis=1, keepdims=True), "tm")
    root = jnp.sqrt(square_sum / samples + 1e-06)
    piece = (values / root).astype(jnp.bfloat16)

    gathered = lax.all_gather(piece, ("chan", "tm"), axis=0, tiled=False)
    gathered = gathered.reshape(chan_parts, tm_parts, channel_rows, local_span)
    whole = gathered.transpose(0, 2, 1, 3).reshape(chan_parts * channel_rows, samples)

    chan_index = lax.axis_index("chan")
    lag_count = LAGS // tm_parts
    lag_base = lax.axis_index("tm") * lag_count
    own = lax.dynamic_slice_in_dim(whole, chan_index * channel_rows, channel_rows, 0)
    reach = LAGS + lag_count
    padded = jnp.pad(own, ((0, 0), (reach, 0)))
    shifted = [
        lax.dynamic_slice_in_dim(padded, reach - lag_base - step, samples, 1)
        for step in range(lag_count)
    ]
    stacked = jnp.concatenate(shifted, axis=0)
    product = lax.dot_general(
        stacked, whole, (((1,), (1,)), ((), ())), preferred_element_type=jnp.float32
    )
    mask_row = lax.dynamic_index_in_dim(block_mask, chan_index, 0, keepdims=False)
    weights = jnp.repeat(mask_row, channel_rows).astype(jnp.float32) * (1.0 / math.sqrt(samples))
    return (product * weights[None, :]).reshape(lag_count, channel_rows, chan_parts * channel_rows)


def solution(mesh):
    placed = (P("chan", "tm"), P(), P())
    return jax.shard_map(
        per_device, mesh=mesh, in_specs=placed, out_specs=P("tm", "chan", None), check_vma=False
    )
```

```python
import math

import jax
import jax.numpy as jnp
from jax import lax
from jax.sharding import PartitionSpec as P

DECIM = 8
TAPS = 64
LAGS = 128


def from_behind(value, axis, steps):
    count = lax.axis_size(axis)
    first, last = (max(0, -steps), min(count, count - steps))
    return lax.ppermute(value, axis, [(source, source + steps) for source in range(first, last)])


def decimate(raw_strain, fir_taps):
    time_span = raw_strain.shape[1]
    margin = TAPS - DECIM
    earlier = from_behind(raw_strain[:, time_span - margin :], "tm", 1)
    extended = jnp.concatenate([earlier, raw_strain], axis=1)
    outputs = time_span // DECIM
    tap_blocks = TAPS // DECIM
    frames = outputs + tap_blocks - 1
    tap_table = fir_taps[::-1].reshape(tap_blocks, DECIM)
    shape_three = (frames, outputs, tap_blocks)
    matches = lax.broadcasted_iota(jnp.int32, shape_three, 0) - lax.broadcasted_iota(
        jnp.int32, shape_three, 1
    ) == lax.broadcasted_iota(jnp.int32, shape_three, 2)
    one_hot = matches.astype(jnp.float32)
    filter_matrix = jnp.einsum("mtj,jr->mrt", one_hot, tap_table, precision=lax.Precision.HIGHEST)
    filter_matrix = filter_matrix.reshape(frames * DECIM, outputs)
    return jnp.dot(
        extended, filter_matrix, precision=lax.Precision.HIGHEST, preferred_element_type=jnp.float32
    )


def per_device(raw_strain, fir_taps, block_mask):
    channel_rows = raw_strain.shape[0]
    chan_parts = lax.axis_size("chan")
    tm_parts = lax.axis_size("tm")
    decimated = decimate(raw_strain, fir_taps)
    rounded = decimated.astype(jnp.bfloat16)
    gathered = lax.all_gather(rounded, "tm", axis=1, tiled=True)
    samples = gathered.shape[1]
    full_values = gathered.astype(jnp.float32)
    root_whole = jnp.sqrt(jnp.mean(full_values * full_values, axis=1, keepdims=True) + 1e-06)
    own = (full_values / root_whole).astype(jnp.bfloat16)
    whole = lax.all_gather(own, "chan", axis=0, tiled=True)

    lag_count = LAGS // tm_parts
    lag_base = lax.axis_index("tm") * lag_count
    reach = LAGS + lag_count
    padded = jnp.pad(own, ((0, 0), (reach, 0)))
    shifted = [
        lax.dynamic_slice_in_dim(padded, reach - lag_base - step, samples, 1)
        for step in range(lag_count)
    ]
    stacked = jnp.concatenate(shifted, axis=0)
    product = lax.dot_general(
        stacked, whole, (((1,), (1,)), ((), ())), preferred_element_type=jnp.float32
    )
    mask_row = lax.dynamic_index_in_dim(block_mask, lax.axis_index("chan"), 0, keepdims=False)
    weights = jnp.repeat(mask_row, channel_rows).astype(jnp.float32) * (1.0 / math.sqrt(samples))
    return (product * weights[None, :]).reshape(lag_count, channel_rows, chan_parts * channel_rows)


def solution(mesh):
    placed = (P("chan", "tm"), P(), P())
    return jax.shard_map(
        per_device, mesh=mesh, in_specs=placed, out_specs=P("tm", "chan", None), check_vma=False
    )
```

```python
import math

import jax
import jax.numpy as jnp
from jax import lax
from jax.sharding import PartitionSpec as P

DECIM = 8
TAPS = 64
LAGS = 128


def from_behind(value, axis, steps):
    count = lax.axis_size(axis)
    first, last = (max(0, -steps), min(count, count - steps))
    return lax.ppermute(value, axis, [(source, source + steps) for source in range(first, last)])


def decimate(raw_strain, fir_taps):
    time_span = raw_strain.shape[1]
    margin = TAPS - DECIM
    earlier = from_behind(raw_strain[:, time_span - margin :], "tm", 1)
    extended = jnp.concatenate([earlier, raw_strain], axis=1)
    outputs = time_span // DECIM
    tap_blocks = TAPS // DECIM
    frames = outputs + tap_blocks - 1
    tap_table = fir_taps[::-1].reshape(tap_blocks, DECIM)
    shape_three = (frames, outputs, tap_blocks)
    matches = lax.broadcasted_iota(jnp.int32, shape_three, 0) - lax.broadcasted_iota(
        jnp.int32, shape_three, 1
    ) == lax.broadcasted_iota(jnp.int32, shape_three, 2)
    one_hot = matches.astype(jnp.float32)
    filter_matrix = jnp.einsum("mtj,jr->mrt", one_hot, tap_table, precision=lax.Precision.HIGHEST)
    filter_matrix = filter_matrix.reshape(frames * DECIM, outputs)
    return jnp.dot(
        extended, filter_matrix, precision=lax.Precision.HIGHEST, preferred_element_type=jnp.float32
    )


def gather_time(piece, parts):
    arrived = [piece] + [
        lax.ppermute(piece, "tm", [(source, (source - shift) % parts) for source in range(parts)])
        for shift in range(1, parts)
    ]
    by_shift = jnp.stack(arrived, axis=0)
    in_order = jnp.roll(by_shift, lax.axis_index("tm"), axis=0)
    return in_order.transpose(1, 0, 2).reshape(piece.shape[0], parts * piece.shape[1])


def per_device(raw_strain, fir_taps, block_mask):
    channel_rows = raw_strain.shape[0]
    chan_parts = lax.axis_size("chan")
    tm_parts = lax.axis_size("tm")
    decimated = decimate(raw_strain, fir_taps)
    rounded = decimated.astype(jnp.bfloat16)
    gathered = gather_time(rounded, tm_parts)
    samples = gathered.shape[1]
    full_values = gathered.astype(jnp.float32)
    root_whole = jnp.sqrt(jnp.mean(full_values * full_values, axis=1, keepdims=True) + 1e-06)
    own = (full_values / root_whole).astype(jnp.bfloat16)
    whole = lax.all_gather(own, "chan", axis=0, tiled=True)

    lag_count = LAGS // tm_parts
    lag_base = lax.axis_index("tm") * lag_count
    reach = LAGS + lag_count
    padded = jnp.pad(own, ((0, 0), (reach, 0)))
    shifted = [
        lax.dynamic_slice_in_dim(padded, reach - lag_base - step, samples, 1)
        for step in range(lag_count)
    ]
    stacked = jnp.concatenate(shifted, axis=0)
    product = lax.dot_general(
        stacked, whole, (((1,), (1,)), ((), ())), preferred_element_type=jnp.float32
    )
    mask_row = lax.dynamic_index_in_dim(block_mask, lax.axis_index("chan"), 0, keepdims=False)
    weights = jnp.repeat(mask_row, channel_rows).astype(jnp.float32) * (1.0 / math.sqrt(samples))
    return (product * weights[None, :]).reshape(lag_count, channel_rows, chan_parts * channel_rows)


def solution(mesh):
    placed = (P("chan", "tm"), P(), P())
    return jax.shard_map(
        per_device, mesh=mesh, in_specs=placed, out_specs=P("tm", "chan", None), check_vma=False
    )
```

```python
import math

import jax
import jax.numpy as jnp
from jax import lax
from jax.sharding import PartitionSpec as P

DECIM = 8
TAPS = 64
LAGS = 128


def from_behind(value, axis, steps):
    count = lax.axis_size(axis)
    first, last = (max(0, -steps), min(count, count - steps))
    return lax.ppermute(value, axis, [(source, source + steps) for source in range(first, last)])


def decimate(raw_strain, fir_taps):
    time_span = raw_strain.shape[1]
    margin = TAPS - DECIM
    earlier = from_behind(raw_strain[:, time_span - margin :], "tm", 1)
    extended = jnp.concatenate([earlier, raw_strain], axis=1)
    outputs = time_span // DECIM
    tap_blocks = TAPS // DECIM
    frames = outputs + tap_blocks - 1
    tap_table = fir_taps[::-1].reshape(tap_blocks, DECIM)
    shape_three = (frames, outputs, tap_blocks)
    matches = lax.broadcasted_iota(jnp.int32, shape_three, 0) - lax.broadcasted_iota(
        jnp.int32, shape_three, 1
    ) == lax.broadcasted_iota(jnp.int32, shape_three, 2)
    one_hot = matches.astype(jnp.float32)
    filter_matrix = jnp.einsum("mtj,jr->mrt", one_hot, tap_table, precision=lax.Precision.HIGHEST)
    filter_matrix = filter_matrix.reshape(frames * DECIM, outputs)
    return jnp.dot(
        extended, filter_matrix, precision=lax.Precision.HIGHEST, preferred_element_type=jnp.float32
    )


def gather_time(piece, parts):
    repeated = jnp.broadcast_to(piece[None], (parts,) + piece.shape)
    in_order = lax.all_to_all(repeated, "tm", 0, 0, tiled=False)
    return in_order.transpose(1, 0, 2).reshape(piece.shape[0], parts * piece.shape[1])


def per_device(raw_strain, fir_taps, block_mask):
    channel_rows = raw_strain.shape[0]
    chan_parts = lax.axis_size("chan")
    tm_parts = lax.axis_size("tm")
    decimated = decimate(raw_strain, fir_taps)
    rounded = decimated.astype(jnp.bfloat16)
    gathered = gather_time(rounded, tm_parts)
    samples = gathered.shape[1]
    full_values = gathered.astype(jnp.float32)
    root_whole = jnp.sqrt(jnp.mean(full_values * full_values, axis=1, keepdims=True) + 1e-06)
    own = (full_values / root_whole).astype(jnp.bfloat16)
    whole = lax.all_gather(own, "chan", axis=0, tiled=True)

    lag_count = LAGS // tm_parts
    lag_base = lax.axis_index("tm") * lag_count
    reach = LAGS + lag_count
    padded = jnp.pad(own, ((0, 0), (reach, 0)))
    shifted = [
        lax.dynamic_slice_in_dim(padded, reach - lag_base - step, samples, 1)
        for step in range(lag_count)
    ]
    stacked = jnp.concatenate(shifted, axis=0)
    product = lax.dot_general(
        stacked, whole, (((1,), (1,)), ((), ())), preferred_element_type=jnp.float32
    )
    mask_row = lax.dynamic_index_in_dim(block_mask, lax.axis_index("chan"), 0, keepdims=False)
    weights = jnp.repeat(mask_row, channel_rows).astype(jnp.float32) * (1.0 / math.sqrt(samples))
    return (product * weights[None, :]).reshape(lag_count, channel_rows, chan_parts * channel_rows)


def solution(mesh):
    placed = (P("chan", "tm"), P(), P())
    return jax.shard_map(
        per_device, mesh=mesh, in_specs=placed, out_specs=P("tm", "chan", None), check_vma=False
    )
```

```python
import functools
import math

import jax
import jax.numpy as jnp
from jax import lax
from jax.experimental import pallas as pl
from jax.experimental.pallas import tpu as pltpu
from jax.sharding import PartitionSpec as P

DECIM = 8
TAPS = 64
LAGS = 128


def from_behind(value, axis, steps):
    count = lax.axis_size(axis)
    first, last = (max(0, -steps), min(count, count - steps))
    return lax.ppermute(value, axis, [(source, source + steps) for source in range(first, last)])


def decimate(raw_strain, fir_taps):
    time_span = raw_strain.shape[1]
    margin = TAPS - DECIM
    earlier = from_behind(raw_strain[:, time_span - margin :], "tm", 1)
    extended = jnp.concatenate([earlier, raw_strain], axis=1)
    outputs = time_span // DECIM
    tap_blocks = TAPS // DECIM
    frames = outputs + tap_blocks - 1
    tap_table = fir_taps[::-1].reshape(tap_blocks, DECIM)
    shape_three = (frames, outputs, tap_blocks)
    matches = lax.broadcasted_iota(jnp.int32, shape_three, 0) - lax.broadcasted_iota(
        jnp.int32, shape_three, 1
    ) == lax.broadcasted_iota(jnp.int32, shape_three, 2)
    one_hot = matches.astype(jnp.float32)
    filter_matrix = jnp.einsum("mtj,jr->mrt", one_hot, tap_table, precision=lax.Precision.HIGHEST)
    filter_matrix = filter_matrix.reshape(frames * DECIM, outputs)
    return jnp.dot(
        extended, filter_matrix, precision=lax.Precision.HIGHEST, preferred_element_type=jnp.float32
    )


def gather_time(piece, parts):
    repeated = jnp.broadcast_to(piece[None], (parts,) + piece.shape)
    in_order = lax.all_to_all(repeated, "tm", 0, 0, tiled=False)
    return in_order.transpose(1, 0, 2).reshape(piece.shape[0], parts * piece.shape[1])


def correlate_kernel(mask_ref, stacked_ref, whole_ref, out_ref, *, scale, block_cols, mask_cols):
    col = pl.program_id(0)
    groups = block_cols // mask_cols
    flags = [mask_ref[col * groups + group] for group in range(groups)]
    live = flags[0] != 0
    for flag in flags[1:]:
        live = jnp.logical_or(live, flag != 0)

    @pl.when(live)
    def _():
        product = lax.dot_general(
            stacked_ref[...], whole_ref[...], (((1,), (1,)), ((), ())),
            preferred_element_type=jnp.float32,
        )
        which = lax.broadcasted_iota(jnp.int32, (1, block_cols), 1) // mask_cols
        weight = jnp.zeros((1, block_cols), jnp.float32)
        for group, flag in enumerate(flags):
            weight = jnp.where(which == group, flag.astype(jnp.float32) * scale, weight)
        out_ref[...] = product * weight

    @pl.when(jnp.logical_not(live))
    def _():
        out_ref[...] = jnp.zeros_like(out_ref)


def correlate(stacked, whole, mask_row, scale, mask_cols):
    rows, depth = stacked.shape
    cols = whole.shape[0]
    block_cols = 256
    kernel = functools.partial(
        correlate_kernel, scale=scale, block_cols=block_cols, mask_cols=mask_cols
    )
    return pl.pallas_call(
        kernel,
        out_shape=jax.ShapeDtypeStruct((rows, cols), jnp.float32),
        grid_spec=pltpu.PrefetchScalarGridSpec(
            num_scalar_prefetch=1,
            grid=(cols // block_cols,),
            in_specs=[
                pl.BlockSpec((rows, depth), lambda col, mask: (0, 0)),
                pl.BlockSpec((block_cols, depth), lambda col, mask: (col, 0)),
            ],
            out_specs=pl.BlockSpec((rows, block_cols), lambda col, mask: (0, col)),
        ),
        cost_estimate=pl.CostEstimate(
            flops=2 * rows * depth * cols,
            bytes_accessed=2 * rows * depth + 2 * cols * depth + 4 * rows * cols,
            transcendentals=0,
        ),
    )(mask_row, stacked, whole)


def per_device(raw_strain, fir_taps, block_mask):
    channel_rows = raw_strain.shape[0]
    chan_parts = lax.axis_size("chan")
    tm_parts = lax.axis_size("tm")
    decimated = decimate(raw_strain, fir_taps)
    rounded = decimated.astype(jnp.bfloat16)
    gathered = gather_time(rounded, tm_parts)
    samples = gathered.shape[1]
    full_values = gathered.astype(jnp.float32)
    root_whole = jnp.sqrt(jnp.mean(full_values * full_values, axis=1, keepdims=True) + 1e-06)
    own = (full_values / root_whole).astype(jnp.bfloat16)
    whole = lax.all_gather(own, "chan", axis=0, tiled=True)

    lag_count = LAGS // tm_parts
    lag_base = lax.axis_index("tm") * lag_count
    reach = LAGS + lag_count
    padded = jnp.pad(own, ((0, 0), (reach, 0)))
    shifted = [
        lax.dynamic_slice_in_dim(padded, reach - lag_base - step, samples, 1)
        for step in range(lag_count)
    ]
    stacked = jnp.concatenate(shifted, axis=0)
    mask_row = lax.dynamic_index_in_dim(block_mask, lax.axis_index("chan"), 0, keepdims=False)
    product = correlate(stacked, whole, mask_row, 1.0 / math.sqrt(samples), channel_rows)
    return product.reshape(lag_count, channel_rows, chan_parts * channel_rows)


def solution(mesh):
    placed = (P("chan", "tm"), P(), P())
    return jax.shard_map(
        per_device, mesh=mesh, in_specs=placed, out_specs=P("tm", "chan", None), check_vma=False
    )
```

```python
import math

import jax
import jax.numpy as jnp
from jax import lax
from jax.sharding import PartitionSpec as P

DECIM = 8
TAPS = 64
LAGS = 128


def filter_matrix_of(fir_taps, outputs):
    tap_blocks = TAPS // DECIM
    frames = outputs + tap_blocks - 1
    tap_table = fir_taps[::-1].reshape(tap_blocks, DECIM)
    shape_three = (frames, outputs, tap_blocks)
    matches = lax.broadcasted_iota(jnp.int32, shape_three, 0) - lax.broadcasted_iota(
        jnp.int32, shape_three, 1
    ) == lax.broadcasted_iota(jnp.int32, shape_three, 2)
    one_hot = matches.astype(jnp.float32)
    filter_matrix = jnp.einsum("mtj,jr->mrt", one_hot, tap_table, precision=lax.Precision.HIGHEST)
    return filter_matrix.reshape(frames * DECIM, outputs)


def decimate_parts(raw_strain, fir_taps):
    time_span = raw_strain.shape[1]
    margin = TAPS - DECIM
    outputs = time_span // DECIM
    filter_matrix = filter_matrix_of(fir_taps, outputs)
    main = jnp.dot(
        raw_strain, filter_matrix[margin:], precision=lax.Precision.HIGHEST,
        preferred_element_type=jnp.float32,
    )
    carry = jnp.dot(
        raw_strain[:, time_span - margin :], filter_matrix[:margin, :DECIM],
        precision=lax.Precision.HIGHEST, preferred_element_type=jnp.float32,
    )
    return main, carry


def gather_time(main, carry, parts):
    piece = jnp.concatenate([main, carry], axis=1)
    repeated = jnp.broadcast_to(piece[None], (parts,) + piece.shape)
    arrived = lax.all_to_all(repeated, "tm", 0, 0, tiled=False)
    span = main.shape[1]
    mains = arrived[:, :, :span]
    carries = arrived[:, :, span:]
    before = jnp.concatenate([jnp.zeros_like(carries[:1]), carries[:-1]], axis=0)
    before = jnp.pad(before, ((0, 0), (0, 0), (0, span - carries.shape[2])))
    decimated = mains + before
    return decimated.transpose(1, 0, 2).reshape(main.shape[0], parts * span)


def per_device(raw_strain, fir_taps, block_mask):
    channel_rows = raw_strain.shape[0]
    chan_parts = lax.axis_size("chan")
    tm_parts = lax.axis_size("tm")
    main, carry = decimate_parts(raw_strain, fir_taps)
    decimated = gather_time(main, carry, tm_parts)
    full_values = lax.reduce_precision(decimated, exponent_bits=8, mantissa_bits=7)
    samples = full_values.shape[1]
    root_whole = jnp.sqrt(jnp.mean(full_values * full_values, axis=1, keepdims=True) + 1e-06)
    own = (full_values / root_whole).astype(jnp.bfloat16)
    whole = lax.all_gather(own, "chan", axis=0, tiled=True)

    lag_count = LAGS // tm_parts
    lag_base = lax.axis_index("tm") * lag_count
    reach = LAGS + lag_count
    padded = jnp.pad(own, ((0, 0), (reach, 0)))
    shifted = [
        lax.dynamic_slice_in_dim(padded, reach - lag_base - step, samples, 1)
        for step in range(lag_count)
    ]
    stacked = jnp.concatenate(shifted, axis=0)
    product = lax.dot_general(
        stacked, whole, (((1,), (1,)), ((), ())), preferred_element_type=jnp.float32
    )
    mask_row = lax.dynamic_index_in_dim(block_mask, lax.axis_index("chan"), 0, keepdims=False)
    weights = jnp.repeat(mask_row, channel_rows).astype(jnp.float32) * (1.0 / math.sqrt(samples))
    return (product * weights[None, :]).reshape(lag_count, channel_rows, chan_parts * channel_rows)


def solution(mesh):
    placed = (P("chan", "tm"), P(), P())
    return jax.shard_map(
        per_device, mesh=mesh, in_specs=placed, out_specs=P("tm", "chan", None), check_vma=False
    )
```

```python
import math

import jax
import jax.numpy as jnp
from jax import lax
from jax.sharding import PartitionSpec as P

DECIM = 8
TAPS = 64
LAGS = 128


def from_behind(value, axis, steps):
    count = lax.axis_size(axis)
    first, last = (max(0, -steps), min(count, count - steps))
    return lax.ppermute(value, axis, [(source, source + steps) for source in range(first, last)])


def decimate(raw_strain, fir_taps):
    time_span = raw_strain.shape[1]
    margin = TAPS - DECIM
    earlier = from_behind(raw_strain[:, time_span - margin :], "tm", 1)
    outputs = time_span // DECIM
    tap_blocks = TAPS // DECIM
    frames = outputs + tap_blocks - 1
    tap_table = fir_taps[::-1].reshape(tap_blocks, DECIM)
    shape_three = (frames, outputs, tap_blocks)
    matches = lax.broadcasted_iota(jnp.int32, shape_three, 0) - lax.broadcasted_iota(
        jnp.int32, shape_three, 1
    ) == lax.broadcasted_iota(jnp.int32, shape_three, 2)
    one_hot = matches.astype(jnp.float32)
    filter_matrix = jnp.einsum("mtj,jr->mrt", one_hot, tap_table, precision=lax.Precision.HIGHEST)
    filter_matrix = filter_matrix.reshape(frames * DECIM, outputs)
    main = jnp.dot(
        raw_strain, filter_matrix[margin:], precision=lax.Precision.HIGHEST,
        preferred_element_type=jnp.float32,
    )
    head = jnp.dot(
        earlier, filter_matrix[:margin, :DECIM], precision=lax.Precision.HIGHEST,
        preferred_element_type=jnp.float32,
    )
    main = lax.optimization_barrier(main)
    return main + jnp.pad(head, ((0, 0), (0, outputs - DECIM)))


def gather_time(piece, parts):
    repeated = jnp.broadcast_to(piece[None], (parts,) + piece.shape)
    in_order = lax.all_to_all(repeated, "tm", 0, 0, tiled=False)
    return in_order.transpose(1, 0, 2).reshape(piece.shape[0], parts * piece.shape[1])


def per_device(raw_strain, fir_taps, block_mask):
    channel_rows = raw_strain.shape[0]
    chan_parts = lax.axis_size("chan")
    tm_parts = lax.axis_size("tm")
    decimated = decimate(raw_strain, fir_taps)
    rounded = decimated.astype(jnp.bfloat16)
    gathered = gather_time(rounded, tm_parts)
    samples = gathered.shape[1]
    full_values = gathered.astype(jnp.float32)
    root_whole = jnp.sqrt(jnp.mean(full_values * full_values, axis=1, keepdims=True) + 1e-06)
    own = (full_values / root_whole).astype(jnp.bfloat16)
    whole = lax.all_gather(own, "chan", axis=0, tiled=True)

    lag_count = LAGS // tm_parts
    lag_base = lax.axis_index("tm") * lag_count
    reach = LAGS + lag_count
    padded = jnp.pad(own, ((0, 0), (reach, 0)))
    shifted = [
        lax.dynamic_slice_in_dim(padded, reach - lag_base - step, samples, 1)
        for step in range(lag_count)
    ]
    stacked = jnp.concatenate(shifted, axis=0)
    product = lax.dot_general(
        stacked, whole, (((1,), (1,)), ((), ())), preferred_element_type=jnp.float32
    )
    mask_row = lax.dynamic_index_in_dim(block_mask, lax.axis_index("chan"), 0, keepdims=False)
    weights = jnp.repeat(mask_row, channel_rows).astype(jnp.float32) * (1.0 / math.sqrt(samples))
    return (product * weights[None, :]).reshape(lag_count, channel_rows, chan_parts * channel_rows)


def solution(mesh):
    placed = (P("chan", "tm"), P(), P())
    return jax.shard_map(
        per_device, mesh=mesh, in_specs=placed, out_specs=P("tm", "chan", None), check_vma=False
    )
```

```python
import math

import jax
import numpy as np
import jax.numpy as jnp
from jax import lax
from jax.sharding import PartitionSpec as P

DECIM = 8
TAPS = 64
LAGS = 128


def from_behind(value, axis, steps):
    count = lax.axis_size(axis)
    first, last = (max(0, -steps), min(count, count - steps))
    return lax.ppermute(value, axis, [(source, source + steps) for source in range(first, last)])


def decimate(raw_strain, fir_taps):
    time_span = raw_strain.shape[1]
    margin = TAPS - DECIM
    earlier = from_behind(raw_strain[:, time_span - margin :], "tm", 1)
    outputs = time_span // DECIM
    tap_blocks = TAPS // DECIM
    frames = outputs + tap_blocks - 1
    tap_grid = fir_taps.reshape(tap_blocks, DECIM)
    shape_three = (frames, outputs, tap_blocks)
    matches = lax.broadcasted_iota(jnp.int32, shape_three, 0) - lax.broadcasted_iota(
        jnp.int32, shape_three, 1
    ) == tap_blocks - 1 - lax.broadcasted_iota(jnp.int32, shape_three, 2)
    one_hot = matches.astype(jnp.float32)
    flip = jnp.asarray(np.eye(DECIM, dtype=np.float32)[::-1])
    tap_table = jnp.dot(tap_grid, flip, precision=lax.Precision.HIGHEST)
    filter_matrix = jnp.einsum("mta,ar->mrt", one_hot, tap_table, precision=lax.Precision.HIGHEST)
    filter_matrix = filter_matrix.reshape(frames * DECIM, outputs)
    main = jnp.dot(
        raw_strain, filter_matrix[margin:], precision=lax.Precision.HIGHEST,
        preferred_element_type=jnp.float32,
    )
    head = jnp.dot(
        earlier, filter_matrix[:margin, :DECIM], precision=lax.Precision.HIGHEST,
        preferred_element_type=jnp.float32,
    )
    main = lax.optimization_barrier(main)
    return main + jnp.pad(head, ((0, 0), (0, outputs - DECIM)))


def gather_time(piece, parts):
    repeated = jnp.broadcast_to(piece[None], (parts,) + piece.shape)
    in_order = lax.all_to_all(repeated, "tm", 0, 0, tiled=False)
    return in_order.transpose(1, 0, 2).reshape(piece.shape[0], parts * piece.shape[1])


def per_device(raw_strain, fir_taps, block_mask):
    channel_rows = raw_strain.shape[0]
    chan_parts = lax.axis_size("chan")
    tm_parts = lax.axis_size("tm")
    decimated = decimate(raw_strain, fir_taps)
    rounded = decimated.astype(jnp.bfloat16)
    gathered = gather_time(rounded, tm_parts)
    samples = gathered.shape[1]
    full_values = gathered.astype(jnp.float32)
    root_whole = jnp.sqrt(jnp.mean(full_values * full_values, axis=1, keepdims=True) + 1e-06)
    own = (full_values / root_whole).astype(jnp.bfloat16)
    whole = lax.all_gather(own, "chan", axis=0, tiled=True)

    lag_count = LAGS // tm_parts
    lag_base = lax.axis_index("tm") * lag_count
    reach = LAGS + lag_count
    padded = jnp.pad(own, ((0, 0), (reach, 0)))
    shifted = [
        lax.dynamic_slice_in_dim(padded, reach - lag_base - step, samples, 1)
        for step in range(lag_count)
    ]
    stacked = jnp.concatenate(shifted, axis=0)
    product = lax.dot_general(
        stacked, whole, (((1,), (1,)), ((), ())), preferred_element_type=jnp.float32
    )
    mask_row = lax.dynamic_index_in_dim(block_mask, lax.axis_index("chan"), 0, keepdims=False)
    weights = jnp.repeat(mask_row, channel_rows).astype(jnp.float32) * (1.0 / math.sqrt(samples))
    return (product * weights[None, :]).reshape(lag_count, channel_rows, chan_parts * channel_rows)


def solution(mesh):
    placed = (P("chan", "tm"), P(), P())
    return jax.shard_map(
        per_device, mesh=mesh, in_specs=placed, out_specs=P("tm", "chan", None), check_vma=False
    )
```

```python
import math

import jax
import jax.numpy as jnp
from jax import lax
from jax.sharding import PartitionSpec as P

DECIM = 8
TAPS = 64
LAGS = 128


def from_behind(value, axis, steps):
    count = lax.axis_size(axis)
    first, last = (max(0, -steps), min(count, count - steps))
    return lax.ppermute(value, axis, [(source, source + steps) for source in range(first, last)])


def decimate(raw_strain, fir_taps):
    time_span = raw_strain.shape[1]
    margin = TAPS - DECIM
    earlier = from_behind(raw_strain, "tm", 1)[:, time_span - margin :]
    outputs = time_span // DECIM
    tap_blocks = TAPS // DECIM
    frames = outputs + tap_blocks - 1
    tap_table = fir_taps[::-1].reshape(tap_blocks, DECIM)
    shape_three = (frames, outputs, tap_blocks)
    matches = lax.broadcasted_iota(jnp.int32, shape_three, 0) - lax.broadcasted_iota(
        jnp.int32, shape_three, 1
    ) == lax.broadcasted_iota(jnp.int32, shape_three, 2)
    one_hot = matches.astype(jnp.float32)
    filter_matrix = jnp.einsum("mtj,jr->mrt", one_hot, tap_table, precision=lax.Precision.HIGHEST)
    filter_matrix = filter_matrix.reshape(frames * DECIM, outputs)
    main = jnp.dot(
        raw_strain, filter_matrix[margin:], precision=lax.Precision.HIGHEST,
        preferred_element_type=jnp.float32,
    )
    head = jnp.dot(
        earlier, filter_matrix[:margin, :DECIM], precision=lax.Precision.HIGHEST,
        preferred_element_type=jnp.float32,
    )
    main = lax.optimization_barrier(main)
    return main + jnp.pad(head, ((0, 0), (0, outputs - DECIM)))


def gather_time(piece, parts):
    repeated = jnp.broadcast_to(piece[None], (parts,) + piece.shape)
    in_order = lax.all_to_all(repeated, "tm", 0, 0, tiled=False)
    return in_order.transpose(1, 0, 2).reshape(piece.shape[0], parts * piece.shape[1])


def per_device(raw_strain, fir_taps, block_mask):
    channel_rows = raw_strain.shape[0]
    chan_parts = lax.axis_size("chan")
    tm_parts = lax.axis_size("tm")
    decimated = decimate(raw_strain, fir_taps)
    rounded = decimated.astype(jnp.bfloat16)
    gathered = gather_time(rounded, tm_parts)
    samples = gathered.shape[1]
    full_values = gathered.astype(jnp.float32)
    root_whole = jnp.sqrt(jnp.mean(full_values * full_values, axis=1, keepdims=True) + 1e-06)
    own = (full_values / root_whole).astype(jnp.bfloat16)
    whole = lax.all_gather(own, "chan", axis=0, tiled=True)

    lag_count = LAGS // tm_parts
    lag_base = lax.axis_index("tm") * lag_count
    reach = LAGS + lag_count
    padded = jnp.pad(own, ((0, 0), (reach, 0)))
    shifted = [
        lax.dynamic_slice_in_dim(padded, reach - lag_base - step, samples, 1)
        for step in range(lag_count)
    ]
    stacked = jnp.concatenate(shifted, axis=0)
    product = lax.dot_general(
        stacked, whole, (((1,), (1,)), ((), ())), preferred_element_type=jnp.float32
    )
    mask_row = lax.dynamic_index_in_dim(block_mask, lax.axis_index("chan"), 0, keepdims=False)
    weights = jnp.repeat(mask_row, channel_rows).astype(jnp.float32) * (1.0 / math.sqrt(samples))
    return (product * weights[None, :]).reshape(lag_count, channel_rows, chan_parts * channel_rows)


def solution(mesh):
    placed = (P("chan", "tm"), P(), P())
    return jax.shard_map(
        per_device, mesh=mesh, in_specs=placed, out_specs=P("tm", "chan", None), check_vma=False
    )
```
